512 devices in a mesh: space: 32 (over y, x_lo, core), modes: 16 (over z, x_hi).
Axes of the slice: x: 4 (x_hi: 2, x_lo: 2; x = x_hi * 2 + x_lo), y: 8, z: 8, core: 2. Of those that a mesh axis runs over, the one named last changes fastest.
Arguments:
- rhs: bfloat16 [2, 256, 512, 512], P(None, 'modes', 'space'), may hold values from -6 to 6
- initial: bfloat16 [2, 256, 512, 512], P(None, 'modes', 'space'), may hold values from -6 to 6
- region: int32 [512, 512], P('space'), may hold values from 0 to 7
- base_table: float32 [2, 8], replicated, may hold values from 0.5 to 4
- term_table: float32 [2, 3, 8], replicated, may hold values from -0.3 to 0.3
- galerkin: bfloat16 [3, 256, 256], replicated, may hold values from -0.375 to 0.375
- block_mask: int32 [3, 16, 16], replicated, may hold values from 0 to 1, as said below
- block_inverse: float32 [16, 16, 16], P('modes'), as said below
Outputs:
- solution: float32 [2, 256, 512, 512], P(None, 'modes', 'space')
The draws below stay inside these ranges and needn't reach their ends.
Inputs may be any that keep to these rules, and one draw needn't show every extreme that they name: `block_mask`: each mode block is coupled with itself by every term, and some pairs of mode blocks are not coupled. `block_inverse`: blocks near the identity, off-diagonal entries at most 0.3 in magnitude.
All inputs are finite; a program needn't handle non-finite values.
Results may differ from the reference program's by a relative error of at most 0.0017.
Values may be sent and summed in bfloat16 or wider, within the bound.
No kernel may reach another device: no remote copies, remote signals or barrier semaphores. Data moves between devices by JAX's collectives and lax.ppermute only.
A program may use at most 64 MiB of HBM per device.

```python
import math
import jax
import jax.numpy as jnp
from jax import lax

FIELDS = 2
P_SIZE = 256
NK = 3
TB = 16
REGIONS = 8
SWEEPS = 2
NY = 512
NBK = 16
NX = 512


def draw_block_mask(key, part):
    key_rows = jax.random.fold_in(key, 11)
    key_cells = jax.random.fold_in(key, 12)
    density = jax.random.randint(key_rows, (NK, NBK, 1), 2, 9)
    cells = jax.random.randint(key_cells, (NK, NBK, NBK), 0, 8)
    mask = jnp.where(cells < density, 1, 0)
    rows = jnp.arange(NBK)[:, None]
    cols = jnp.arange(NBK)[None, :]
    mask = jnp.where(rows == cols, 1, mask)
    mask = jnp.where(cols == (rows + 1) % NBK, 0, mask)
    return mask.astype(jnp.int32)


def draw_block_inverse(key, part):
    key_noise = jax.random.fold_in(key, 21)
    noise = jnp.clip(jax.random.normal(key_noise, (NBK, TB, TB), jnp.float32), -4.0, 4.0)
    eye = (jnp.arange(TB)[:, None] == jnp.arange(TB)[None, :]).astype(jnp.float32)
    return eye[None] + 0.3 / TB ** 0.5 * noise


def plant(result, rng, low, largest):
    place = [jax.random.randint(jax.random.fold_in(rng, axis), (), 0, length) for axis, length in enumerate(result.shape)]
    main_axis = result.shape.index(max(result.shape))
    beside = place[:main_axis] + [(place[main_axis] + 1) % result.shape[main_axis]] + place[main_axis + 1:]
    return result.at[tuple(place)].set(low).at[tuple(beside)].set(largest)


def level_of(stream_key, dims, split, low, largest):
    def one(axis_at, blocks):
        heights = jax.random.uniform(jax.random.fold_in(jax.random.fold_in(stream_key, 6), axis_at), (blocks,), jnp.float32, low / len(split), largest / len(split))
        return jnp.repeat(jnp.exp(heights), dims[axis_at] // blocks).reshape((-1,) + (1,) * (len(dims) - axis_at - 1))

    loudness = one(*split[0])
    for cut in split[1:]:
        loudness = loudness * one(*cut)
    return loudness


def centred(own_key, dims, width, most, split=(), dtype=jnp.bfloat16):
    values = width * jax.random.normal(own_key, dims, jnp.float32)
    if split:
        values = values * level_of(own_key, dims, split, -0.22, 0.18)
    return jnp.clip(values, -most, most).astype(dtype)


def setup_inputs(seed: int = 0) -> dict:
    splits = jax.random.split(jax.random.key(seed), 9)
    rhs = centred(splits[0], (FIELDS, P_SIZE, NX, NY), 1.0, 6.0, ((1, 16), (2, 32)))
    initial = centred(splits[1], (FIELDS, P_SIZE, NX, NY), 1.0, 6.0, ((1, 16), (2, 32)))
    region = plant(jax.random.randint(splits[2], (NX, NY), 0, REGIONS), jax.random.fold_in(splits[2], 1), 0, REGIONS - 1).astype(jnp.int32)
    base_table = jnp.clip(jnp.exp(jax.random.uniform(splits[3], (FIELDS, REGIONS), jnp.float32, math.log(0.5), math.log(4.0))), 0.5, 4.0)
    term_table = jnp.clip(jax.random.uniform(splits[4], (FIELDS, NK, REGIONS), jnp.float32, -0.3, 0.3), -0.3, 0.3)
    galerkin = centred(splits[5], (NK, P_SIZE, P_SIZE), P_SIZE ** -0.5, 0.375)
    block_mask = draw_block_mask(jax.random.fold_in(splits[8], 71), 0)
    block_inverse = draw_block_inverse(jax.random.fold_in(splits[8], 71), 0)
    return {"rhs": rhs, "initial": initial, "region": region, "base_table": base_table, "term_table": term_table, "galerkin": galerkin, "block_mask": block_mask, "block_inverse": block_inverse}


def lookup(table, region):
    total = jnp.zeros(table.shape[:-1] + region.shape, jnp.float32)
    for which in range(REGIONS):
        total = total + table[..., which, None, None] * (region == which).astype(jnp.float32)
    return total


def laplace(field):
    upper = jnp.roll(field, -1, -2)
    lower = jnp.roll(field, 1, -2)
    zeros = jnp.zeros(field.shape[:-1] + (1,), jnp.float32)
    right = jnp.concatenate([field[..., 1:], zeros], -1)
    left = jnp.concatenate([zeros, field[..., :-1]], -1)
    return 4.0 * field - upper - lower - right - left


def reference(rhs, initial, region, base_table, term_table, galerkin, block_mask, block_inverse):
    shaped = galerkin.reshape(NK, NBK, TB, NBK, TB)
    coupling = (shaped * block_mask[:, :, None, :, None].astype(jnp.bfloat16)).reshape(NK, P_SIZE, P_SIZE)

    def one_field(items):
        rhs_f, init_f, base_f, term_f = items
        base = lookup(base_f, region)
        coef = lookup(term_f, region)
        u_field = init_f.astype(jnp.float32)
        for sweep in range(SWEEPS):
            rounded = lax.optimization_barrier(u_field.astype(jnp.bfloat16)).astype(jnp.float32)
            lap_rounded = laplace(rounded)
            coupled = jnp.zeros((P_SIZE, NX * NY), jnp.float32)
            for term in range(NK):
                tiles = (coef[term][None] * lap_rounded).astype(jnp.bfloat16)
                coupled = coupled + jnp.dot(coupling[term], tiles.reshape(P_SIZE, NX * NY), preferred_element_type=jnp.float32)
            coupled = lax.optimization_barrier(coupled.astype(jnp.bfloat16)).astype(jnp.float32).reshape(P_SIZE, NX, NY)
            resid = rhs_f.astype(jnp.float32) - base[None] * laplace(u_field) - coupled
            scaled = (resid / (4.0 * base[None])).reshape(NBK, TB, NX, NY)
            update = jnp.einsum("bac,bcxy->baxy", block_inverse, scaled, precision=lax.Precision.HIGHEST)
            u_field = u_field + 0.6 * update.reshape(P_SIZE, NX, NY)
        return u_field

    return lax.map(one_field, (rhs, initial, base_table, term_table))
```

```python
import jax
import jax.numpy as jnp
from jax import lax
from jax.sharding import PartitionSpec as P

SWEEPS = 2


def with_halo(block, sides, width):
    for axis, dim in sides:
        count = lax.axis_size(axis)
        forward = [(i, i + 1) for i in range(count - 1)]
        forward.append((count - 1, 0))
        backward = [(target, source) for source, target in forward]
        low = lax.ppermute(
            lax.slice_in_dim(block, block.shape[dim] - width, None, axis=dim), axis, forward
        )
        high = lax.ppermute(lax.slice_in_dim(block, 0, width, axis=dim), axis, backward)
        block = jnp.concatenate([low, block, high], axis=dim)
    return block


def lookup(table, region):
    total = jnp.zeros(table.shape[:-1] + region.shape, jnp.float32)
    for which in range(table.shape[-1]):
        total = total + table[..., which, None, None] * (region == which).astype(jnp.float32)
    return total


def laplace_padded(padded):
    center = padded[..., 1:-1, :]
    zeros = jnp.zeros(center.shape[:-1] + (1,), jnp.float32)
    right = jnp.concatenate([center[..., 1:], zeros], -1)
    left = jnp.concatenate([zeros, center[..., :-1]], -1)
    return 4.0 * center - padded[..., 2:, :] - padded[..., :-2, :] - right - left


def laplace_full_pad(padded):
    center = padded[..., 1:-1, 1:-1]
    return (
        4.0 * center
        - padded[..., 2:, 1:-1]
        - padded[..., :-2, 1:-1]
        - padded[..., 1:-1, 2:]
        - padded[..., 1:-1, :-2]
    )


def body(rhs, initial, region, base_table, term_table, galerkin, block_mask, block_inverse):
    terms = galerkin.shape[0]
    modes_all = galerkin.shape[1]
    blocks = block_mask.shape[1]
    width = modes_all // blocks
    shaped = galerkin.reshape(terms, blocks, width, blocks, width)
    coupling = (shaped * block_mask[:, :, None, :, None].astype(jnp.bfloat16)).reshape(
        terms, modes_all, modes_all
    )
    base = lookup(base_table, region)
    coef = lookup(term_table, region)
    chunks = lax.axis_size("modes")
    cols = region.shape[-1]
    chunk_w = cols // chunks
    me = lax.axis_index("modes")
    coef_chunk = lax.dynamic_slice_in_dim(coef, me * chunk_w, chunk_w, axis=-1)
    rhs_float = rhs.astype(jnp.float32)
    inverse_base = 1.0 / (4.0 * base[:, None])
    u_field = initial.astype(jnp.float32)
    for sweep in range(SWEEPS):
        padded = with_halo(u_field, (("space", 2),), 1)
        local = base[:, None] * laplace_padded(padded)
        rounded = padded.astype(jnp.bfloat16)
        rounded = jnp.pad(rounded, ((0, 0), (0, 0), (0, 0), (1, 1)))
        pieces = jnp.stack(
            [rounded[..., c * chunk_w : c * chunk_w + chunk_w + 2] for c in range(chunks)], axis=3
        )
        gathered = lax.all_to_all(pieces, "modes", split_axis=3, concat_axis=1, tiled=True)
        gathered = gathered[:, :, :, 0, :].astype(jnp.float32)
        lap_rounded = laplace_full_pad(gathered)
        tiles = (coef_chunk[:, :, None] * lap_rounded[:, None]).astype(jnp.bfloat16)
        mixed = jnp.einsum(
            "kij,fkjxy->fixy", coupling, tiles, preferred_element_type=jnp.float32
        ).astype(jnp.bfloat16)
        coupled = lax.all_to_all(mixed, "modes", split_axis=1, concat_axis=3, tiled=True)
        resid = rhs_float - local - coupled.astype(jnp.float32)
        scaled = resid * inverse_base
        fields, modes_dev, cells_x, cells_y = scaled.shape
        grouped = scaled.reshape(fields, modes_dev // width, width, cells_x, cells_y)
        update = jnp.einsum(
            "bac,fbcxy->fbaxy", block_inverse, grouped, precision=lax.Precision.HIGHEST
        )
        u_field = u_field + 0.6 * update.reshape(fields, modes_dev, cells_x, cells_y)
    return u_field


def solution(mesh):
    in_specs = (
        P(None, "modes", "space", None),
        P(None, "modes", "space", None),
        P("space", None),
        P(),
        P(),
        P(),
        P(),
        P("modes", None, None),
    )
    out_specs = P(None, "modes", "space", None)
    return jax.shard_map(body, mesh=mesh, in_specs=in_specs, out_specs=out_specs, check_vma=False)
```

```python
import jax
import jax.numpy as jnp
from jax import lax
from jax.sharding import PartitionSpec as P

SWEEPS = 2
LANES = 128


def ring_halo(block, axis, dim):
    count = lax.axis_size(axis)
    forward = [(i, (i + 1) % count) for i in range(count)]
    backward = [(target, source) for source, target in forward]
    low = lax.ppermute(lax.slice_in_dim(block, block.shape[dim] - 1, None, axis=dim), axis, forward)
    high = lax.ppermute(lax.slice_in_dim(block, 0, 1, axis=dim), axis, backward)
    return jnp.concatenate([low, block, high], axis=dim)


def lookup(table, region):
    total = jnp.zeros(table.shape[:-1] + region.shape, jnp.float32)
    for which in range(table.shape[-1]):
        total = total + table[..., which, None, None] * (region == which).astype(jnp.float32)
    return total


def shift_lanes(center, fill_left, fill_right):
    right = jnp.concatenate([center[..., 1:], fill_right[..., None]], -1)
    left = jnp.concatenate([fill_left[..., None], center[..., :-1]], -1)
    return right, left


def body(rhs, initial, region, base_table, term_table, galerkin, block_mask, block_inverse):
    terms = galerkin.shape[0]
    modes_all = galerkin.shape[1]
    blocks = block_mask.shape[1]
    width = modes_all // blocks
    shaped = galerkin.reshape(terms, blocks, width, blocks, width)
    coupling = (shaped * block_mask[:, :, None, :, None].astype(jnp.bfloat16)).reshape(
        terms, modes_all, modes_all
    )
    coupling = coupling.transpose(1, 0, 2).reshape(modes_all, terms * modes_all)

    fields = rhs.shape[0]
    rows, cols = region.shape
    devs = lax.axis_size("modes")
    col_chunks = cols // LANES
    row_chunks = devs // col_chunks
    rows_c = rows // row_chunks
    me = lax.axis_index("modes")
    my_r = me // col_chunks
    my_c = me % col_chunks

    base = lookup(base_table, region)[:, :, None, :]
    coef = lookup(term_table, region)
    coef_chunk = lax.dynamic_slice(
        coef, (0, 0, my_r * rows_c, my_c * LANES), (fields, terms, rows_c, LANES)
    )
    coef_chunk = coef_chunk.transpose(0, 2, 1, 3)[:, :, :, None, :]
    rhs_x = rhs.transpose(0, 2, 1, 3).astype(jnp.float32)
    inverse_base = 1.0 / (4.0 * base)
    u_field = initial.transpose(0, 2, 1, 3).astype(jnp.float32)
    inv = block_inverse[0]
    zero_col = jnp.zeros(u_field.shape[:1] + (rows_c,) + u_field.shape[2:3], jnp.bfloat16)
    for sweep in range(SWEEPS):
        padded = ring_halo(u_field, "space", 1)
        center = padded[:, 1:-1]
        zeros = jnp.zeros(center.shape[:-1], jnp.float32)
        right, left = shift_lanes(center, zeros, zeros)
        local = base * (4.0 * center - padded[:, 2:] - padded[:, :-2] - right - left)

        rounded = padded.astype(jnp.bfloat16)
        pieces = []
        for r in range(row_chunks):
            for c in range(col_chunks):
                main = rounded[:, r * rows_c : r * rows_c + rows_c + 2, :, c * LANES : (c + 1) * LANES]
                inner = rounded[:, r * rows_c + 1 : r * rows_c + rows_c + 1]
                hl = inner[..., c * LANES - 1] if c > 0 else zero_col
                hr = inner[..., (c + 1) * LANES] if c < col_chunks - 1 else zero_col
                side = jnp.concatenate([hl, hr], axis=1).transpose(0, 2, 1)
                side = jnp.pad(side, ((0, 0), (0, 0), (0, LANES - 2 * rows_c)))[:, None]
                pieces.append(jnp.concatenate([main, side], axis=1))
        stacked = jnp.stack(pieces, axis=2)
        got = lax.all_to_all(stacked, "modes", split_axis=2, concat_axis=3, tiled=True)
        got = got[:, :, 0].astype(jnp.float32)
        g_center = got[:, 1 : rows_c + 1]
        side = got[:, rows_c + 2]
        g_left = side[..., :rows_c].transpose(0, 2, 1)
        g_right = side[..., rows_c : 2 * rows_c].transpose(0, 2, 1)
        g_r, g_l = shift_lanes(g_center, g_left, g_right)
        lap = 4.0 * g_center - got[:, 2 : rows_c + 2] - got[:, 0:rows_c] - g_r - g_l
        tiles = (coef_chunk * lap[:, :, None]).astype(jnp.bfloat16)
        tiles = tiles.reshape(fields, rows_c, terms * modes_all, LANES)
        mixed = jnp.einsum(
            "ic,fxcy->fxiy", coupling, tiles, preferred_element_type=jnp.float32
        ).astype(jnp.bfloat16)
        mixed = mixed.reshape(fields, rows_c, devs, modes_all // devs, LANES)
        back = lax.all_to_all(mixed, "modes", split_axis=2, concat_axis=2, tiled=True)
        back = back.reshape(fields, rows_c, row_chunks, col_chunks, -1, LANES)
        coupled = back.transpose(0, 2, 1, 4, 3, 5).reshape(u_field.shape)

        resid = rhs_x - local - coupled.astype(jnp.float32)
        scaled = resid * inverse_base
        update = jnp.einsum("ac,fxcy->fxay", inv, scaled, precision=lax.Precision.HIGHEST)
        u_field = u_field + 0.6 * update
    return u_field.transpose(0, 2, 1, 3)


def solution(mesh):
    in_specs = (
        P(None, "modes", "space", None),
        P(None, "modes", "space", None),
        P("space", None),
        P(),
        P(),
        P(),
        P(),
        P("modes", None, None),
    )
    out_specs = P(None, "modes", "space", None)
    return jax.shard_map(body, mesh=mesh, in_specs=in_specs, out_specs=out_specs, check_vma=False)
```

```python
import jax
import jax.numpy as jnp
from jax import lax
from jax.sharding import PartitionSpec as P

SWEEPS = 2
LANES = 128


def ring_halo(block, axis, dim):
    count = lax.axis_size(axis)
    forward = [(i, (i + 1) % count) for i in range(count)]
    backward = [(target, source) for source, target in forward]
    low = lax.ppermute(lax.slice_in_dim(block, block.shape[dim] - 1, None, axis=dim), axis, forward)
    high = lax.ppermute(lax.slice_in_dim(block, 0, 1, axis=dim), axis, backward)
    return jnp.concatenate([low, block, high], axis=dim)


def lookup(table, region):
    total = jnp.zeros(table.shape[:-1] + region.shape, jnp.float32)
    for which in range(table.shape[-1]):
        total = total + table[..., which, None, None] * (region == which).astype(jnp.float32)
    return total


def laplace_rows(padded, fill_left, fill_right):
    center = padded[:, 1:-1]
    right = jnp.concatenate([center[..., 1:], fill_right[..., None]], -1)
    left = jnp.concatenate([fill_left[..., None], center[..., :-1]], -1)
    return 4.0 * center - padded[:, 2:] - padded[:, :-2] - right - left


def body(rhs, initial, region, base_table, term_table, galerkin, block_mask, block_inverse):
    terms = galerkin.shape[0]
    modes_all = galerkin.shape[1]
    blocks = block_mask.shape[1]
    width = modes_all // blocks
    shaped = galerkin.reshape(terms, blocks, width, blocks, width)
    coupling = (shaped * block_mask[:, :, None, :, None].astype(jnp.bfloat16)).reshape(
        terms, modes_all, modes_all
    )
    coupling = coupling.transpose(1, 0, 2).reshape(modes_all, terms * modes_all)

    fields, modes_dev = rhs.shape[:2]
    rows, cols = region.shape
    devs = lax.axis_size("modes")
    spaces = lax.axis_size("space")
    col_chunks = cols // LANES
    row_chunks = devs // col_chunks
    rows_c = rows // row_chunks
    me = lax.axis_index("modes")
    my_r = me // col_chunks
    my_c = me % col_chunks

    every = lax.all_gather(block_inverse, "modes", tiled=True)
    eye = jnp.eye(blocks, dtype=jnp.float32)
    dense_inv = (every[:, :, None, :] * eye[:, None, :, None]).reshape(modes_all, modes_all)

    base = lax.dynamic_slice(
        lookup(base_table, region), (0, my_r * rows_c, my_c * LANES), (fields, rows_c, LANES)
    )[:, :, None, :]
    coef = lax.dynamic_slice(
        lookup(term_table, region),
        (0, 0, my_r * rows_c, my_c * LANES),
        (fields, terms, rows_c, LANES),
    )
    coef = coef.transpose(0, 2, 1, 3)[:, :, :, None, :]
    inverse_base = 1.0 / (4.0 * base)

    rhs_p = rhs.reshape(fields, modes_dev, row_chunks, rows_c, col_chunks, LANES)
    rhs_p = rhs_p.transpose(0, 3, 2, 4, 1, 5).reshape(fields, rows_c, devs, modes_dev, LANES)
    rhs_c = lax.all_to_all(rhs_p, "modes", split_axis=2, concat_axis=3, tiled=True)[:, :, 0]
    rhs_c = rhs_c.astype(jnp.float32)

    init_x = ring_halo(initial.transpose(0, 2, 1, 3), "space", 1)
    zero_col = jnp.zeros((fields, rows_c, modes_dev), init_x.dtype)
    pieces = []
    for r in range(row_chunks):
        for c in range(col_chunks):
            main = init_x[:, r * rows_c : r * rows_c + rows_c + 2, :, c * LANES : (c + 1) * LANES]
            inner = init_x[:, r * rows_c + 1 : r * rows_c + rows_c + 1]
            hl = inner[..., c * LANES - 1] if c > 0 else zero_col
            hr = inner[..., (c + 1) * LANES] if c < col_chunks - 1 else zero_col
            side = jnp.concatenate([hl, hr], axis=1).transpose(0, 2, 1)
            side = jnp.pad(side, ((0, 0), (0, 0), (0, LANES - 2 * rows_c)))[:, None]
            pieces.append(jnp.concatenate([main, side], axis=1))
    stacked = jnp.stack(pieces, axis=2)
    got = lax.all_to_all(stacked, "modes", split_axis=2, concat_axis=3, tiled=True)[:, :, 0]
    got = got.astype(jnp.float32)
    side = got[:, rows_c + 2]
    fill_l = side[..., :rows_c].transpose(0, 2, 1)
    fill_r = side[..., rows_c : 2 * rows_c].transpose(0, 2, 1)
    padded = got[:, : rows_c + 2]
    u_field = padded[:, 1:-1]

    flat = ("space", "modes")
    total_rc = spaces * row_chunks

    def dev_of(g, c):
        s, r = divmod(g % total_rc, row_chunks)
        return s * devs + r * col_chunks + c

    down = [(dev_of(g, c), dev_of(g + 1, c)) for g in range(total_rc) for c in range(col_chunks)]
    up = [(b, a) for a, b in down]
    rightward = [
        (s * devs + r * col_chunks + c, s * devs + r * col_chunks + c + 1)
        for s in range(spaces)
        for r in range(row_chunks)
        for c in range(col_chunks - 1)
    ]
    leftward = [(b, a) for a, b in rightward]

    for sweep in range(SWEEPS):
        if sweep > 0:
            low = lax.ppermute(u_field[:, -1:], flat, down)
            high = lax.ppermute(u_field[:, :1], flat, up)
            fill_l = lax.ppermute(u_field[..., -1], flat, rightward)
            fill_r = lax.ppermute(u_field[..., 0], flat, leftward)
            padded = jnp.concatenate([low, u_field, high], axis=1)
        lap = laplace_rows(padded, fill_l, fill_r)
        local = base * lap
        if sweep > 0:
            lap_r = laplace_rows(
                padded.astype(jnp.bfloat16).astype(jnp.float32),
                fill_l.astype(jnp.bfloat16).astype(jnp.float32),
                fill_r.astype(jnp.bfloat16).astype(jnp.float32),
            )
        else:
            lap_r = lap
        tiles = (coef * lap_r[:, :, None]).astype(jnp.bfloat16)
        tiles = tiles.reshape(fields, rows_c, terms * modes_all, LANES)
        coupled = jnp.einsum(
            "ic,fxcy->fxiy", coupling, tiles, preferred_element_type=jnp.float32
        ).astype(jnp.bfloat16)
        resid = rhs_c - local - coupled.astype(jnp.float32)
        scaled = resid * inverse_base
        update = jnp.einsum("ij,fxjy->fxiy", dense_inv, scaled, precision=lax.Precision.HIGHEST)
        u_field = u_field + 0.6 * update

    out = u_field.reshape(fields, rows_c, devs, modes_dev, LANES)
    back = lax.all_to_all(out, "modes", split_axis=2, concat_axis=2, tiled=True)
    back = back.reshape(fields, rows_c, row_chunks, col_chunks, modes_dev, LANES)
    return back.transpose(0, 4, 2, 1, 3, 5).reshape(fields, modes_dev, rows, cols)


def solution(mesh):
    in_specs = (
        P(None, "modes", "space", None),
        P(None, "modes", "space", None),
        P("space", None),
        P(),
        P(),
        P(),
        P(),
        P("modes", None, None),
    )
    out_specs = P(None, "modes", "space", None)
    return jax.shard_map(body, mesh=mesh, in_specs=in_specs, out_specs=out_specs, check_vma=False)
```

```python
import jax
import jax.numpy as jnp
from jax import lax
from jax.sharding import PartitionSpec as P

SWEEPS = 2
LANES = 128


def ring_halo(block, axis, dim):
    count = lax.axis_size(axis)
    forward = [(i, (i + 1) % count) for i in range(count)]
    backward = [(target, source) for source, target in forward]
    low = lax.ppermute(lax.slice_in_dim(block, block.shape[dim] - 1, None, axis=dim), axis, forward)
    high = lax.ppermute(lax.slice_in_dim(block, 0, 1, axis=dim), axis, backward)
    return jnp.concatenate([low, block, high], axis=dim)


def lookup(table, region):
    total = jnp.zeros(table.shape[:-1] + region.shape, jnp.float32)
    for which in range(table.shape[-1]):
        total = total + table[..., which, None, None] * (region == which).astype(jnp.float32)
    return total


def laplace_rows(padded, fill_left, fill_right):
    center = padded[1:-1]
    right = jnp.concatenate([center[..., 1:], fill_right[..., None]], -1)
    left = jnp.concatenate([fill_left[..., None], center[..., :-1]], -1)
    return 4.0 * center - padded[2:] - padded[:-2] - right - left


def body(rhs, initial, region, base_table, term_table, galerkin, block_mask, block_inverse):
    terms = galerkin.shape[0]
    modes_all = galerkin.shape[1]
    blocks = block_mask.shape[1]
    width = modes_all // blocks
    shaped = galerkin.reshape(terms, blocks, width, blocks, width)
    coupling = (shaped * block_mask[:, :, None, :, None].astype(jnp.bfloat16)).reshape(
        terms, modes_all, modes_all
    )
    coupling = coupling.transpose(1, 0, 2).reshape(modes_all, terms * modes_all)

    fields, modes_dev = rhs.shape[:2]
    rows, cols = region.shape
    devs = lax.axis_size("modes")
    spaces = lax.axis_size("space")
    col_chunks = cols // LANES
    row_chunks = devs // col_chunks
    rows_c = rows // row_chunks
    me = lax.axis_index("modes")
    my_r = me // col_chunks
    my_c = me % col_chunks

    every = lax.all_to_all(
        jnp.broadcast_to(block_inverse, (devs,) + block_inverse.shape[1:]),
        "modes", split_axis=0, concat_axis=0, tiled=True,
    )
    eye = jnp.eye(blocks, dtype=jnp.float32)
    dense_inv = (every[:, :, None, :] * eye[:, None, :, None]).reshape(modes_all, modes_all)

    base = lax.dynamic_slice(
        lookup(base_table, region), (0, my_r * rows_c, my_c * LANES), (fields, rows_c, LANES)
    )[:, :, None, :]
    coef = lax.dynamic_slice(
        lookup(term_table, region),
        (0, 0, my_r * rows_c, my_c * LANES),
        (fields, terms, rows_c, LANES),
    )
    coef = coef.transpose(0, 2, 1, 3)[:, :, :, None, :]
    inverse_base = 1.0 / (4.0 * base)

    init_x = ring_halo(initial.transpose(0, 2, 1, 3), "space", 1)

    flat = ("space", "modes")
    total_rc = spaces * row_chunks

    def dev_of(g, c):
        s, r = divmod(g % total_rc, row_chunks)
        return s * devs + r * col_chunks + c

    down = [(dev_of(g, c), dev_of(g + 1, c)) for g in range(total_rc) for c in range(col_chunks)]
    up = [(b, a) for a, b in down]
    rightward = [
        (s * devs + r * col_chunks + c, s * devs + r * col_chunks + c + 1)
        for s in range(spaces)
        for r in range(row_chunks)
        for c in range(col_chunks - 1)
    ]
    leftward = [(b, a) for a, b in rightward]

    def pack(init_f, rhs_f):
        top = init_f[0 : rows : rows_c]
        mid = init_f[1 : rows + 1].reshape(row_chunks, rows_c, modes_dev, cols)
        bot = init_f[rows_c + 1 : rows + 2 : rows_c]
        main = jnp.concatenate([top[:, None], mid, bot[:, None]], axis=1)
        main = main.reshape(row_chunks, rows_c + 2, modes_dev, col_chunks, LANES)
        inner = init_f[1 : rows + 1]
        hl = jnp.pad(inner[..., LANES - 1 : cols - 1 : LANES], ((0, 0), (0, 0), (1, 0)))
        hr = jnp.pad(inner[..., LANES : cols : LANES], ((0, 0), (0, 0), (0, 1)))
        sides = []
        for h in (hl, hr):
            sides.append(h.reshape(row_chunks, rows_c, modes_dev, col_chunks).transpose(0, 2, 3, 1))
        side = jnp.concatenate(sides, axis=-1)
        side = jnp.pad(side, ((0, 0), (0, 0), (0, 0), (0, LANES - 2 * rows_c)))[:, None]
        rp = rhs_f.reshape(modes_dev, row_chunks, rows_c, col_chunks, LANES).transpose(1, 2, 0, 3, 4)
        full = jnp.concatenate([main, side, rp], axis=1)
        full = full.transpose(0, 3, 1, 2, 4).reshape(devs, -1, modes_dev, LANES)
        return lax.all_to_all(full, "modes", split_axis=0, concat_axis=2, tiled=True)[0]

    outs = []
    for f in range(fields):
        got = pack(init_x[f], rhs[f])
        padded = got[: rows_c + 2].astype(jnp.float32)
        side = got[rows_c + 2].astype(jnp.float32)
        fill_l = side[:, :rows_c].T
        fill_r = side[:, rows_c : 2 * rows_c].T
        rhs_c = got[rows_c + 3 :].astype(jnp.float32)
        u_field = padded[1:-1]
        for sweep in range(SWEEPS):
            if sweep > 0:
                low = lax.ppermute(u_field[-1:], flat, down)
                high = lax.ppermute(u_field[:1], flat, up)
                fill_l = lax.ppermute(u_field[..., -1], flat, rightward)
                fill_r = lax.ppermute(u_field[..., 0], flat, leftward)
                padded = jnp.concatenate([low, u_field, high], axis=0)
            lap = laplace_rows(padded, fill_l, fill_r)
            local = base[f] * lap
            if sweep > 0:
                lap_r = laplace_rows(
                    padded.astype(jnp.bfloat16).astype(jnp.float32),
                    fill_l.astype(jnp.bfloat16).astype(jnp.float32),
                    fill_r.astype(jnp.bfloat16).astype(jnp.float32),
                )
            else:
                lap_r = lap
            tiles = (coef[f] * lap_r[:, None]).astype(jnp.bfloat16)
            tiles = tiles.reshape(rows_c, terms * modes_all, LANES)
            coupled = jnp.einsum(
                "ic,xcy->xiy", coupling, tiles, preferred_element_type=jnp.float32
            ).astype(jnp.bfloat16)
            resid = rhs_c - local - coupled.astype(jnp.float32)
            scaled = resid * inverse_base[f]
            update = jnp.einsum("ij,xjy->xiy", dense_inv, scaled, precision=lax.Precision.HIGHEST)
            u_field = u_field + 0.6 * update
        out = u_field.reshape(rows_c, devs, modes_dev, LANES)
        back = lax.all_to_all(out, "modes", split_axis=1, concat_axis=1, tiled=True)
        back = back.reshape(rows_c, row_chunks, col_chunks, modes_dev, LANES)
        outs.append(back.transpose(3, 1, 0, 2, 4).reshape(modes_dev, rows, cols))
    return jnp.stack(outs)


def solution(mesh):
    in_specs = (
        P(None, "modes", "space", None),
        P(None, "modes", "space", None),
        P("space", None),
        P(),
        P(),
        P(),
        P(),
        P("modes", None, None),
    )
    out_specs = P(None, "modes", "space", None)
    return jax.shard_map(body, mesh=mesh, in_specs=in_specs, out_specs=out_specs, check_vma=False)
```

```python
import jax
import jax.numpy as jnp
from jax import lax
from jax.sharding import PartitionSpec as P

SWEEPS = 2
LANES = 128


def ring_halo(block, axis, dim):
    count = lax.axis_size(axis)
    forward = [(i, (i + 1) % count) for i in range(count)]
    backward = [(target, source) for source, target in forward]
    low = lax.ppermute(lax.slice_in_dim(block, block.shape[dim] - 1, None, axis=dim), axis, forward)
    high = lax.ppermute(lax.slice_in_dim(block, 0, 1, axis=dim), axis, backward)
    return jnp.concatenate([low, block, high], axis=dim)


def lookup(table, region):
    total = jnp.zeros(table.shape[:-1] + region.shape, jnp.float32)
    for which in range(table.shape[-1]):
        total = total + table[..., which, None, None] * (region == which).astype(jnp.float32)
    return total


def laplace_rows(padded, fill_left, fill_right):
    center = padded[:, 1:-1]
    right = jnp.concatenate([center[..., 1:], fill_right[..., None]], -1)
    left = jnp.concatenate([fill_left[..., None], center[..., :-1]], -1)
    return 4.0 * center - padded[:, 2:] - padded[:, :-2] - right - left


def body(rhs, initial, region, base_table, term_table, galerkin, block_mask, block_inverse):
    terms = galerkin.shape[0]
    modes_all = galerkin.shape[1]
    blocks = block_mask.shape[1]
    width = modes_all // blocks
    shaped = galerkin.reshape(terms, blocks, width, blocks, width)
    coupling = (shaped * block_mask[:, :, None, :, None].astype(jnp.bfloat16)).reshape(
        terms, modes_all, modes_all
    )
    coupling = coupling.transpose(1, 0, 2).reshape(modes_all, terms * modes_all)

    fields, modes_dev = rhs.shape[:2]
    rows, cols = region.shape
    devs = lax.axis_size("modes")
    spaces = lax.axis_size("space")
    col_chunks = cols // LANES
    row_chunks = devs // col_chunks
    rows_c = rows // row_chunks
    me = lax.axis_index("modes")
    my_r = me // col_chunks
    my_c = me % col_chunks

    every = lax.all_to_all(
        jnp.broadcast_to(block_inverse, (devs,) + block_inverse.shape[1:]),
        "modes", split_axis=0, concat_axis=0, tiled=True,
    )
    eye = jnp.eye(blocks, dtype=jnp.float32)
    dense_inv = (every[:, :, None, :] * eye[:, None, :, None]).reshape(modes_all, modes_all)

    base = lax.dynamic_slice(
        lookup(base_table, region), (0, my_r * rows_c, my_c * LANES), (fields, rows_c, LANES)
    )[:, :, None, :]
    coef = lax.dynamic_slice(
        lookup(term_table, region),
        (0, 0, my_r * rows_c, my_c * LANES),
        (fields, terms, rows_c, LANES),
    )
    coef = coef.transpose(0, 2, 1, 3)[:, :, :, None, :]
    inverse_base = 1.0 / (4.0 * base)

    init_x = ring_halo(initial.transpose(0, 2, 1, 3), "space", 1)

    flat = ("space", "modes")
    total_rc = spaces * row_chunks

    def dev_of(g, c):
        s, r = divmod(g % total_rc, row_chunks)
        return s * devs + r * col_chunks + c

    down = [(dev_of(g, c), dev_of(g + 1, c)) for g in range(total_rc) for c in range(col_chunks)]
    up = [(b, a) for a, b in down]
    rightward = [
        (s * devs + r * col_chunks + c, s * devs + r * col_chunks + c + 1)
        for s in range(spaces)
        for r in range(row_chunks)
        for c in range(col_chunks - 1)
    ]
    leftward = [(b, a) for a, b in rightward]

    def pack(init_f, rhs_f):
        top = init_f[:, 0 : rows : rows_c]
        mid = init_f[:, 1 : rows + 1].reshape(fields, row_chunks, rows_c, modes_dev, cols)
        bot = init_f[:, rows_c + 1 : rows + 2 : rows_c]
        main = jnp.concatenate([top[:, :, None], mid, bot[:, :, None]], axis=2)
        main = main.reshape(fields, row_chunks, rows_c + 2, modes_dev, col_chunks, LANES)
        inner = init_f[:, 1 : rows + 1]
        hl = jnp.pad(inner[..., LANES - 1 : cols - 1 : LANES], ((0, 0), (0, 0), (0, 0), (1, 0)))
        hr = jnp.pad(inner[..., LANES : cols : LANES], ((0, 0), (0, 0), (0, 0), (0, 1)))
        sides = []
        for h in (hl, hr):
            h = h.reshape(fields, row_chunks, rows_c, modes_dev, col_chunks)
            sides.append(h.transpose(0, 1, 3, 4, 2))
        side = jnp.concatenate(sides, axis=-1)
        side = jnp.pad(side, ((0, 0),) * 4 + ((0, LANES - 2 * rows_c),))[:, :, None]
        rp = rhs_f.reshape(fields, modes_dev, row_chunks, rows_c, col_chunks, LANES)
        rp = rp.transpose(0, 2, 3, 1, 4, 5)
        full = jnp.concatenate([main, side, rp], axis=2)
        full = full.transpose(1, 4, 0, 2, 3, 5).reshape(devs, fields, -1, modes_dev, LANES)
        return lax.all_to_all(full, "modes", split_axis=0, concat_axis=3, tiled=True)[0]

    got = pack(init_x, rhs)
    padded = got[:, : rows_c + 2].astype(jnp.float32)
    side = got[:, rows_c + 2].astype(jnp.float32)
    fill_l = side[..., :rows_c].transpose(0, 2, 1)
    fill_r = side[..., rows_c : 2 * rows_c].transpose(0, 2, 1)
    rhs_c = got[:, rows_c + 3 :].astype(jnp.float32)
    u_field = padded[:, 1:-1]
    for sweep in range(SWEEPS):
        if sweep > 0:
            low = lax.ppermute(u_field[:, -1:], flat, down)
            high = lax.ppermute(u_field[:, :1], flat, up)
            fill_l = lax.ppermute(u_field[..., -1], flat, rightward)
            fill_r = lax.ppermute(u_field[..., 0], flat, leftward)
            padded = jnp.concatenate([low, u_field, high], axis=1)
        lap = laplace_rows(padded, fill_l, fill_r)
        local = base * lap
        if sweep > 0:
            lap_r = laplace_rows(
                padded.astype(jnp.bfloat16).astype(jnp.float32),
                fill_l.astype(jnp.bfloat16).astype(jnp.float32),
                fill_r.astype(jnp.bfloat16).astype(jnp.float32),
            )
        else:
            lap_r = lap
        tiles = (coef * lap_r[:, :, None]).astype(jnp.bfloat16)
        tiles = tiles.reshape(fields, rows_c, terms * modes_all, LANES)
        coupled = jnp.einsum(
            "ic,fxcy->fxiy", coupling, tiles, preferred_element_type=jnp.float32
        ).astype(jnp.bfloat16)
        resid = rhs_c - local - coupled.astype(jnp.float32)
        scaled = resid * inverse_base
        update = jnp.einsum("ij,fxjy->fxiy", dense_inv, scaled, precision=lax.Precision.HIGHEST)
        u_field = u_field + 0.6 * update

    out = u_field.reshape(fields, rows_c, devs, modes_dev, LANES)
    back = lax.all_to_all(out, "modes", split_axis=2, concat_axis=2, tiled=True)
    back = back.reshape(fields, rows_c, row_chunks, col_chunks, modes_dev, LANES)
    return back.transpose(0, 4, 2, 1, 3, 5).reshape(fields, modes_dev, rows, cols)


def solution(mesh):
    in_specs = (
        P(None, "modes", "space", None),
        P(None, "modes", "space", None),
        P("space", None),
        P(),
        P(),
        P(),
        P(),
        P("modes", None, None),
    )
    out_specs = P(None, "modes", "space", None)
    return jax.shard_map(body, mesh=mesh, in_specs=in_specs, out_specs=out_specs, check_vma=False)
```

```python
import jax
import jax.numpy as jnp
from jax import lax
from jax.sharding import PartitionSpec as P

SWEEPS = 2
LANES = 128


def ring_halo(block, axis, dim):
    count = lax.axis_size(axis)
    forward = [(i, (i + 1) % count) for i in range(count)]
    backward = [(target, source) for source, target in forward]
    low = lax.ppermute(lax.slice_in_dim(block, block.shape[dim] - 1, None, axis=dim), axis, forward)
    high = lax.ppermute(lax.slice_in_dim(block, 0, 1, axis=dim), axis, backward)
    return jnp.concatenate([low, block, high], axis=dim)


def lookup(table, region):
    total = jnp.zeros(table.shape[:-1] + region.shape, jnp.float32)
    for which in range(table.shape[-1]):
        total = total + table[..., which, None, None] * (region == which).astype(jnp.float32)
    return total


def laplace_rows(padded, fill_left, fill_right):
    center = padded[:, 1:-1]
    right = jnp.concatenate([center[..., 1:], fill_right[..., None]], -1)
    left = jnp.concatenate([fill_left[..., None], center[..., :-1]], -1)
    return 4.0 * center - padded[:, 2:] - padded[:, :-2] - right - left


def body(rhs, initial, region, base_table, term_table, galerkin, block_mask, block_inverse):
    terms = galerkin.shape[0]
    modes_all = galerkin.shape[1]
    blocks = block_mask.shape[1]
    width = modes_all // blocks
    shaped = galerkin.reshape(terms, blocks, width, blocks, width)
    coupling = (shaped * block_mask[:, :, None, :, None].astype(jnp.bfloat16)).reshape(
        terms, modes_all, modes_all
    )
    coupling = coupling.transpose(1, 0, 2).reshape(modes_all, terms * modes_all)

    fields, modes_dev = rhs.shape[:2]
    rows, cols = region.shape
    devs = lax.axis_size("modes")
    spaces = lax.axis_size("space")
    col_chunks = cols // LANES
    row_chunks = devs // col_chunks
    rows_c = rows // row_chunks
    me = lax.axis_index("modes")
    my_r = me // col_chunks
    my_c = me % col_chunks

    inv_hi = lax.optimization_barrier(block_inverse[0].astype(jnp.bfloat16))
    rest = block_inverse[0] - inv_hi.astype(jnp.float32)
    inv_mid = lax.optimization_barrier(rest.astype(jnp.bfloat16))
    inv_lo = (rest - inv_mid.astype(jnp.float32)).astype(jnp.bfloat16)
    inv_code = jnp.concatenate([inv_hi, inv_mid, inv_lo], axis=-1)

    base = lax.dynamic_slice(
        lookup(base_table, region), (0, my_r * rows_c, my_c * LANES), (fields, rows_c, LANES)
    )[:, :, None, :]
    coef = lax.dynamic_slice(
        lookup(term_table, region),
        (0, 0, my_r * rows_c, my_c * LANES),
        (fields, terms, rows_c, LANES),
    )
    coef = coef.transpose(0, 2, 1, 3)[:, :, :, None, :]
    inverse_base = 1.0 / (4.0 * base)

    rp = rhs.reshape(fields, modes_dev, row_chunks, rows_c, col_chunks, LANES)
    rp = rp.transpose(2, 4, 0, 3, 1, 5).reshape(devs, fields, rows_c, modes_dev, LANES)
    rhs_c = lax.all_to_all(rp, "modes", split_axis=0, concat_axis=3, tiled=True)[0]
    rhs_c = rhs_c.astype(jnp.float32)

    init_x = ring_halo(initial.transpose(0, 2, 1, 3), "space", 1)

    flat = ("space", "modes")
    total_rc = spaces * row_chunks

    def dev_of(g, c):
        s, r = divmod(g % total_rc, row_chunks)
        return s * devs + r * col_chunks + c

    down = [(dev_of(g, c), dev_of(g + 1, c)) for g in range(total_rc) for c in range(col_chunks)]
    up = [(b, a) for a, b in down]
    rightward = [
        (s * devs + r * col_chunks + c, s * devs + r * col_chunks + c + 1)
        for s in range(spaces)
        for r in range(row_chunks)
        for c in range(col_chunks - 1)
    ]
    leftward = [(b, a) for a, b in rightward]

    def pack(init_f, rhs_f):
        top = init_f[:, 0 : rows : rows_c]
        mid = init_f[:, 1 : rows + 1].reshape(fields, row_chunks, rows_c, modes_dev, cols)
        bot = init_f[:, rows_c + 1 : rows + 2 : rows_c]
        main = jnp.concatenate([top[:, :, None], mid, bot[:, :, None]], axis=2)
        main = main.reshape(fields, row_chunks, rows_c + 2, modes_dev, col_chunks, LANES)
        inner = init_f[:, 1 : rows + 1]
        hl = jnp.pad(inner[..., LANES - 1 : cols - 1 : LANES], ((0, 0), (0, 0), (0, 0), (1, 0)))
        hr = jnp.pad(inner[..., LANES : cols : LANES], ((0, 0), (0, 0), (0, 0), (0, 1)))
        sides = []
        for h in (hl, hr):
            h = h.reshape(fields, row_chunks, rows_c, modes_dev, col_chunks)
            sides.append(h.transpose(0, 1, 3, 4, 2))
        code = jnp.broadcast_to(
            inv_code[None, None, :, None, :], sides[0].shape[:-1] + inv_code.shape[-1:]
        )
        side = jnp.concatenate(sides + [code], axis=-1)
        side = jnp.pad(side, ((0, 0),) * 4 + ((0, LANES - side.shape[-1]),))[:, :, None]
        full = jnp.concatenate([main, side], axis=2)
        full = full.transpose(1, 4, 0, 2, 3, 5).reshape(devs, fields, -1, modes_dev, LANES)
        return lax.all_to_all(full, "modes", split_axis=0, concat_axis=3, tiled=True)[0]

    got = pack(init_x, rhs)
    padded = got[:, : rows_c + 2].astype(jnp.float32)
    side = got[:, rows_c + 2].astype(jnp.float32)
    fill_l = side[..., :rows_c].transpose(0, 2, 1)
    fill_r = side[..., rows_c : 2 * rows_c].transpose(0, 2, 1)
    code = side[0, :, 2 * rows_c : 2 * rows_c + 3 * width]
    every = (code[:, :width] + code[:, width : 2 * width]) + code[:, 2 * width :]
    every = every.reshape(blocks, width, width)
    eye = jnp.eye(blocks, dtype=jnp.float32)
    dense_inv = (every[:, :, None, :] * eye[:, None, :, None]).reshape(modes_all, modes_all)
    u_field = padded[:, 1:-1]
    for sweep in range(SWEEPS):
        if sweep > 0:
            low = lax.ppermute(u_field[:, -1:], flat, down)
            high = lax.ppermute(u_field[:, :1], flat, up)
            fill_l = lax.ppermute(u_field[..., -1], flat, rightward)
            fill_r = lax.ppermute(u_field[..., 0], flat, leftward)
            padded = jnp.concatenate([low, u_field, high], axis=1)
        lap = laplace_rows(padded, fill_l, fill_r)
        local = base * lap
        if sweep > 0:
            rounded = lax.optimization_barrier(
                (padded.astype(jnp.bfloat16), fill_l.astype(jnp.bfloat16), fill_r.astype(jnp.bfloat16))
            )
            lap_r = laplace_rows(*(part.astype(jnp.float32) for part in rounded))
        else:
            lap_r = lap
        tiles = (coef * lap_r[:, :, None]).astype(jnp.bfloat16)
        tiles = tiles.reshape(fields, rows_c, terms * modes_all, LANES)
        coupled = jnp.einsum(
            "ic,fxcy->fxiy", coupling, tiles, preferred_element_type=jnp.float32
        ).astype(jnp.bfloat16)
        resid = rhs_c - local - coupled.astype(jnp.float32)
        scaled = resid * inverse_base
        update = jnp.einsum("ij,fxjy->fxiy", dense_inv, scaled, precision=lax.Precision.HIGHEST)
        u_field = u_field + 0.6 * update

    out = u_field.reshape(fields, rows_c, devs, modes_dev, LANES)
    back = lax.all_to_all(out, "modes", split_axis=2, concat_axis=2, tiled=True)
    back = back.reshape(fields, rows_c, row_chunks, col_chunks, modes_dev, LANES)
    return back.transpose(0, 4, 2, 1, 3, 5).reshape(fields, modes_dev, rows, cols)


def solution(mesh):
    in_specs = (
        P(None, "modes", "space", None),
        P(None, "modes", "space", None),
        P("space", None),
        P(),
        P(),
        P(),
        P(),
        P("modes", None, None),
    )
    out_specs = P(None, "modes", "space", None)
    return jax.shard_map(body, mesh=mesh, in_specs=in_specs, out_specs=out_specs, check_vma=False)
```

```python
import jax
import jax.numpy as jnp
from jax import lax
from jax.sharding import PartitionSpec as P

SWEEPS = 2
LANES = 128


def ring_halo(block, axis, dim):
    count = lax.axis_size(axis)
    forward = [(i, (i + 1) % count) for i in range(count)]
    backward = [(target, source) for source, target in forward]
    low = lax.ppermute(lax.slice_in_dim(block, block.shape[dim] - 1, None, axis=dim), axis, forward)
    high = lax.ppermute(lax.slice_in_dim(block, 0, 1, axis=dim), axis, backward)
    return jnp.concatenate([low, block, high], axis=dim)


def lookup(table, region):
    total = jnp.zeros(table.shape[:-1] + region.shape, jnp.float32)
    for which in range(table.shape[-1]):
        total = total + table[..., which, None, None] * (region == which).astype(jnp.float32)
    return total


def laplace_rows(padded, fill_left, fill_right):
    center = padded[:, 1:-1]
    right = jnp.concatenate([center[..., 1:], fill_right[..., None]], -1)
    left = jnp.concatenate([fill_left[..., None], center[..., :-1]], -1)
    return 4.0 * center - padded[:, 2:] - padded[:, :-2] - right - left


def sweeps(rhs, initial, region, base_table, term_table, galerkin, block_mask, block_inverse):
    terms = galerkin.shape[0]
    modes_all = galerkin.shape[1]
    blocks = block_mask.shape[1]
    width = modes_all // blocks
    shaped = galerkin.reshape(terms, blocks, width, blocks, width)
    coupling = (shaped * block_mask[:, :, None, :, None].astype(jnp.bfloat16)).reshape(
        terms, modes_all, modes_all
    )
    coupling = coupling.transpose(1, 0, 2).reshape(modes_all, terms * modes_all)

    fields, modes_dev = rhs.shape[:2]
    rows, cols = region.shape
    devs = lax.axis_size("modes")
    spaces = lax.axis_size("space")
    col_chunks = cols // LANES
    row_chunks = devs // col_chunks
    rows_c = rows // row_chunks
    me = lax.axis_index("modes")
    my_r = me // col_chunks
    my_c = me % col_chunks

    inv_hi = lax.optimization_barrier(block_inverse[0].astype(jnp.bfloat16))
    rest = block_inverse[0] - inv_hi.astype(jnp.float32)
    inv_mid = lax.optimization_barrier(rest.astype(jnp.bfloat16))
    inv_lo = (rest - inv_mid.astype(jnp.float32)).astype(jnp.bfloat16)
    inv_code = jnp.concatenate([inv_hi, inv_mid, inv_lo], axis=-1)

    base = lax.dynamic_slice(
        lookup(base_table, region), (0, my_r * rows_c, my_c * LANES), (fields, rows_c, LANES)
    )[:, :, None, :]
    coef = lax.dynamic_slice(
        lookup(term_table, region),
        (0, 0, my_r * rows_c, my_c * LANES),
        (fields, terms, rows_c, LANES),
    )
    coef = coef.transpose(0, 2, 1, 3)[:, :, :, None, :]
    inverse_base = 1.0 / (4.0 * base)

    rp = rhs.reshape(fields, modes_dev, row_chunks, rows_c, col_chunks, LANES)
    rp = rp.transpose(2, 4, 0, 3, 1, 5).reshape(devs, fields, rows_c, modes_dev, LANES)
    rhs_c = lax.all_to_all(rp, "modes", split_axis=0, concat_axis=3, tiled=True)[0]
    rhs_c = rhs_c.astype(jnp.float32)

    init_x = ring_halo(initial.transpose(0, 2, 1, 3), "space", 1)

    flat = ("space", "modes")
    total_rc = spaces * row_chunks

    def dev_of(g, c):
        s, r = divmod(g % total_rc, row_chunks)
        return s * devs + r * col_chunks + c

    down = [(dev_of(g, c), dev_of(g + 1, c)) for g in range(total_rc) for c in range(col_chunks)]
    up = [(b, a) for a, b in down]
    rightward = [
        (s * devs + r * col_chunks + c, s * devs + r * col_chunks + c + 1)
        for s in range(spaces)
        for r in range(row_chunks)
        for c in range(col_chunks - 1)
    ]
    leftward = [(b, a) for a, b in rightward]

    def pack(init_f):
        top = init_f[:, 0 : rows : rows_c]
        mid = init_f[:, 1 : rows + 1].reshape(fields, row_chunks, rows_c, modes_dev, cols)
        bot = init_f[:, rows_c + 1 : rows + 2 : rows_c]
        main = jnp.concatenate([top[:, :, None], mid, bot[:, :, None]], axis=2)
        main = main.reshape(fields, row_chunks, rows_c + 2, modes_dev, col_chunks, LANES)
        inner = init_f[:, 1 : rows + 1]
        hl = jnp.pad(inner[..., LANES - 1 : cols - 1 : LANES], ((0, 0), (0, 0), (0, 0), (1, 0)))
        hr = jnp.pad(inner[..., LANES : cols : LANES], ((0, 0), (0, 0), (0, 0), (0, 1)))
        sides = []
        for h in (hl, hr):
            h = h.reshape(fields, row_chunks, rows_c, modes_dev, col_chunks)
            sides.append(h.transpose(0, 1, 3, 4, 2))
        code = jnp.broadcast_to(
            inv_code[None, None, :, None, :], sides[0].shape[:-1] + inv_code.shape[-1:]
        )
        side = jnp.concatenate(sides + [code], axis=-1)
        side = jnp.pad(side, ((0, 0),) * 4 + ((0, LANES - side.shape[-1]),))[:, :, None]
        full = jnp.concatenate([main, side], axis=2)
        full = full.transpose(1, 4, 0, 2, 3, 5).reshape(devs, fields, -1, modes_dev, LANES)
        return lax.all_to_all(full, "modes", split_axis=0, concat_axis=3, tiled=True)[0]

    got = pack(init_x)
    padded = got[:, : rows_c + 2].astype(jnp.float32)
    side = got[:, rows_c + 2].astype(jnp.float32)
    fill_l = side[..., :rows_c].transpose(0, 2, 1)
    fill_r = side[..., rows_c : 2 * rows_c].transpose(0, 2, 1)
    code = side[0, :, 2 * rows_c : 2 * rows_c + 3 * width]
    every = (code[:, :width] + code[:, width : 2 * width]) + code[:, 2 * width :]
    every = every.reshape(blocks, width, width)
    eye = jnp.eye(blocks, dtype=jnp.float32)
    dense_inv = (every[:, :, None, :] * eye[:, None, :, None]).reshape(modes_all, modes_all)
    u_field = padded[:, 1:-1]
    for sweep in range(SWEEPS):
        if sweep > 0:
            low = lax.ppermute(u_field[:, -1:], flat, down)
            high = lax.ppermute(u_field[:, :1], flat, up)
            fill_l = lax.ppermute(u_field[..., -1], flat, rightward)
            fill_r = lax.ppermute(u_field[..., 0], flat, leftward)
            padded = jnp.concatenate([low, u_field, high], axis=1)
        lap = laplace_rows(padded, fill_l, fill_r)
        local = base * lap
        if sweep > 0:
            rounded = lax.optimization_barrier(
                (padded.astype(jnp.bfloat16), fill_l.astype(jnp.bfloat16), fill_r.astype(jnp.bfloat16))
            )
            lap_r = laplace_rows(*(part.astype(jnp.float32) for part in rounded))
        else:
            lap_r = lap
        tiles = (coef * lap_r[:, :, None]).astype(jnp.bfloat16)
        tiles = tiles.reshape(fields, rows_c, terms * modes_all, LANES)
        coupled = jnp.einsum(
            "ic,fxcy->fxiy", coupling, tiles, preferred_element_type=jnp.float32
        ).astype(jnp.bfloat16)
        resid = rhs_c - local - coupled.astype(jnp.float32)
        scaled = resid * inverse_base
        update = jnp.einsum("ij,fxjy->fxiy", dense_inv, scaled, precision=lax.Precision.HIGHEST)
        u_field = u_field + 0.6 * update

    out = u_field.reshape(fields, rows_c, devs, modes_dev, LANES)
    back = lax.all_to_all(out, "modes", split_axis=2, concat_axis=2, tiled=True)
    back = back.reshape(fields, rows_c, row_chunks, col_chunks, modes_dev, LANES)
    return back.transpose(0, 4, 2, 1, 3, 5).reshape(fields, modes_dev, rows, cols)


def solution(mesh):
    in_specs = (
        P(None, "modes", "space", None),
        P(None, "modes", "space", None),
        P("space", None),
        P(),
        P(),
        P(),
        P(),
        P("modes", None, None),
    )
    out_specs = P(None, "modes", "space", None)
    return jax.shard_map(sweeps, mesh=mesh, in_specs=in_specs, out_specs=out_specs, check_vma=False)
```

```python
import jax
import jax.numpy as jnp
from jax import lax
from jax.sharding import PartitionSpec as P

SWEEPS = 2
LANES = 128


def ring_halo(block, axis, dim):
    count = lax.axis_size(axis)
    forward = [(i, (i + 1) % count) for i in range(count)]
    backward = [(target, source) for source, target in forward]
    low = lax.ppermute(lax.slice_in_dim(block, block.shape[dim] - 1, None, axis=dim), axis, forward)
    high = lax.ppermute(lax.slice_in_dim(block, 0, 1, axis=dim), axis, backward)
    return jnp.concatenate([low, block, high], axis=dim)


def lookup(table, region):
    total = jnp.zeros(table.shape[:-1] + region.shape, jnp.float32)
    for which in range(table.shape[-1]):
        total = total + table[..., which, None, None] * (region == which).astype(jnp.float32)
    return total


def laplace_rows(padded, fill_left, fill_right):
    center = padded[:, 1:-1]
    right = jnp.concatenate([center[..., 1:], fill_right[..., None]], -1)
    left = jnp.concatenate([fill_left[..., None], center[..., :-1]], -1)
    return 4.0 * center - padded[:, 2:] - padded[:, :-2] - right - left


def sweeps(rhs, initial, region, base_table, term_table, galerkin, block_mask, block_inverse):
    terms = galerkin.shape[0]
    modes_all = galerkin.shape[1]
    blocks = block_mask.shape[1]
    width = modes_all // blocks
    shaped = galerkin.reshape(terms, blocks, width, blocks, width)
    coupling = (shaped * block_mask[:, :, None, :, None].astype(jnp.bfloat16)).reshape(
        terms, modes_all, modes_all
    )
    coupling = coupling.transpose(1, 0, 2).reshape(modes_all, terms * modes_all)

    fields, modes_dev = rhs.shape[:2]
    rows, cols = region.shape
    devs = lax.axis_size("modes")
    spaces = lax.axis_size("space")
    col_chunks = cols // LANES
    row_chunks = devs // col_chunks
    rows_c = rows // row_chunks
    me = lax.axis_index("modes")
    my_r = me // col_chunks
    my_c = me % col_chunks

    inv_hi = lax.optimization_barrier(block_inverse[0].astype(jnp.bfloat16))
    rest = block_inverse[0] - inv_hi.astype(jnp.float32)
    inv_mid = lax.optimization_barrier(rest.astype(jnp.bfloat16))
    inv_lo = (rest - inv_mid.astype(jnp.float32)).astype(jnp.bfloat16)
    inv_code = jnp.concatenate([inv_hi, inv_mid, inv_lo], axis=-1)

    base = lax.dynamic_slice(
        lookup(base_table, region), (0, my_r * rows_c, my_c * LANES), (fields, rows_c, LANES)
    )[:, :, None, :]
    coef = lax.dynamic_slice(
        lookup(term_table, region),
        (0, 0, my_r * rows_c, my_c * LANES),
        (fields, terms, rows_c, LANES),
    )
    coef = coef.transpose(0, 2, 1, 3)[:, :, :, None, :]
    inverse_base = 1.0 / (4.0 * base)

    rp = rhs.reshape(fields, modes_dev, row_chunks, rows_c, col_chunks, LANES)
    rp = rp.transpose(2, 4, 0, 3, 1, 5).reshape(devs, fields, rows_c, modes_dev, LANES)
    rhs_c = lax.all_to_all(rp, "modes", split_axis=0, concat_axis=3, tiled=True)[0]
    rhs_c = rhs_c.astype(jnp.float32)

    init_x = ring_halo(initial.transpose(0, 2, 1, 3), "space", 1)

    flat = ("space", "modes")
    total_rc = spaces * row_chunks

    def dev_of(g, c):
        s, r = divmod(g % total_rc, row_chunks)
        return s * devs + r * col_chunks + c

    down = [(dev_of(g, c), dev_of(g + 1, c)) for g in range(total_rc) for c in range(col_chunks)]
    up = [(b, a) for a, b in down]
    rightward = [
        (s * devs + r * col_chunks + c, s * devs + r * col_chunks + c + 1)
        for s in range(spaces)
        for r in range(row_chunks)
        for c in range(col_chunks - 1)
    ]
    leftward = [(b, a) for a, b in rightward]

    def pack(init_f):
        top = init_f[:, 0 : rows : rows_c]
        mid = init_f[:, 1 : rows + 1].reshape(fields, row_chunks, rows_c, modes_dev, cols)
        bot = init_f[:, rows_c + 1 : rows + 2 : rows_c]
        main = jnp.concatenate([top[:, :, None], mid, bot[:, :, None]], axis=2)
        main = main.reshape(fields, row_chunks, rows_c + 2, modes_dev, col_chunks, LANES)
        inner = init_f[:, 1 : rows + 1]
        hl = jnp.pad(inner[..., LANES - 1 : cols - 1 : LANES], ((0, 0), (0, 0), (0, 0), (1, 0)))
        hr = jnp.pad(inner[..., LANES : cols : LANES], ((0, 0), (0, 0), (0, 0), (0, 1)))
        sides = []
        for h in (hl, hr):
            h = h.reshape(fields, row_chunks, rows_c, modes_dev, col_chunks)
            sides.append(h.transpose(0, 1, 3, 4, 2))
        code = jnp.broadcast_to(
            inv_code[None, None, :, None, :], sides[0].shape[:-1] + inv_code.shape[-1:]
        )
        side = jnp.concatenate(sides + [code], axis=-1)
        side = jnp.pad(side, ((0, 0),) * 4 + ((0, LANES - side.shape[-1]),))[:, :, None]
        full = jnp.concatenate([main, side], axis=2)
        full = full.transpose(1, 4, 0, 2, 3, 5).reshape(devs, fields, -1, modes_dev, LANES)
        return lax.all_to_all(full, "modes", split_axis=0, concat_axis=3, tiled=True)[0]

    got = pack(init_x)
    padded = got[:, : rows_c + 2].astype(jnp.float32)
    side = got[:, rows_c + 2].astype(jnp.float32)
    fill_l = side[..., :rows_c].transpose(0, 2, 1)
    fill_r = side[..., rows_c : 2 * rows_c].transpose(0, 2, 1)
    code = side[0, :, 2 * rows_c : 2 * rows_c + 3 * width]
    every = (code[:, :width] + code[:, width : 2 * width]) + code[:, 2 * width :]
    every = every.reshape(blocks, width, width)
    eye = jnp.eye(blocks, dtype=jnp.float32)
    dense_inv = (every[:, :, None, :] * eye[:, None, :, None]).reshape(modes_all, modes_all)
    u_field = padded[:, 1:-1]

    def to_owner(mixed):
        mixed = mixed.reshape(fields, rows_c, devs, modes_dev, LANES)
        back = lax.all_to_all(mixed, "modes", split_axis=2, concat_axis=2, tiled=True)
        back = back.reshape(fields, rows_c, row_chunks, col_chunks, modes_dev, LANES)
        return back.transpose(0, 2, 1, 4, 3, 5).reshape(fields, rows, modes_dev, cols)

    coupled_owner = []
    for sweep in range(SWEEPS):
        if sweep > 0:
            low = lax.ppermute(u_field[:, -1:], flat, down)
            high = lax.ppermute(u_field[:, :1], flat, up)
            fill_l = lax.ppermute(u_field[..., -1], flat, rightward)
            fill_r = lax.ppermute(u_field[..., 0], flat, leftward)
            padded = jnp.concatenate([low, u_field, high], axis=1)
            rounded = lax.optimization_barrier(
                (padded.astype(jnp.bfloat16), fill_l.astype(jnp.bfloat16), fill_r.astype(jnp.bfloat16))
            )
            lap_r = laplace_rows(*(part.astype(jnp.float32) for part in rounded))
        else:
            lap = laplace_rows(padded, fill_l, fill_r)
            lap_r = lap
        tiles = (coef * lap_r[:, :, None]).astype(jnp.bfloat16)
        tiles = tiles.reshape(fields, rows_c, terms * modes_all, LANES)
        coupled = jnp.einsum(
            "ic,fxcy->fxiy", coupling, tiles, preferred_element_type=jnp.float32
        ).astype(jnp.bfloat16)
        coupled_owner.append(to_owner(coupled))
        if sweep < SWEEPS - 1:
            resid = rhs_c - base * lap - coupled.astype(jnp.float32)
            scaled = resid * inverse_base
            update = jnp.einsum(
                "ij,fxjy->fxiy", dense_inv, scaled, precision=lax.Precision.HIGHEST
            )
            u_field = u_field + 0.6 * update

    base_o = lookup(base_table, region)[:, :, None, :]
    inv_base_o = 1.0 / (4.0 * base_o)
    rhs_o = rhs.transpose(0, 2, 1, 3).astype(jnp.float32)
    own_inv = block_inverse[0]
    pad_o = init_x.astype(jnp.float32)
    u_o = pad_o[:, 1:-1]
    zeros = jnp.zeros(u_o.shape[:-1], jnp.float32)
    for sweep in range(SWEEPS):
        if sweep > 0:
            pad_o = ring_halo(u_o, "space", 1)
        lap_o = laplace_rows(pad_o, zeros, zeros)
        resid = rhs_o - base_o * lap_o - coupled_owner[sweep].astype(jnp.float32)
        scaled = resid * inv_base_o
        update = jnp.einsum("ac,fxcy->fxay", own_inv, scaled, precision=lax.Precision.HIGHEST)
        u_o = u_o + 0.6 * update
    return u_o.transpose(0, 2, 1, 3)


def solution(mesh):
    in_specs = (
        P(None, "modes", "space", None),
        P(None, "modes", "space", None),
        P("space", None),
        P(),
        P(),
        P(),
        P(),
        P("modes", None, None),
    )
    out_specs = P(None, "modes", "space", None)
    return jax.shard_map(sweeps, mesh=mesh, in_specs=in_specs, out_specs=out_specs, check_vma=False)
```

```python
import jax
import jax.numpy as jnp
from jax import lax
from jax.sharding import PartitionSpec as P

SWEEPS = 2
LANES = 128


def ring_halo(block, axis, dim):
    count = lax.axis_size(axis)
    forward = [(i, (i + 1) % count) for i in range(count)]
    backward = [(target, source) for source, target in forward]
    low = lax.ppermute(lax.slice_in_dim(block, block.shape[dim] - 1, None, axis=dim), axis, forward)
    high = lax.ppermute(lax.slice_in_dim(block, 0, 1, axis=dim), axis, backward)
    return jnp.concatenate([low, block, high], axis=dim)


def lookup(table, region):
    total = jnp.zeros(table.shape[:-1] + region.shape, jnp.float32)
    for which in range(table.shape[-1]):
        total = total + table[..., which, None, None] * (region == which).astype(jnp.float32)
    return total


def laplace_rows(padded, fill_left, fill_right):
    center = padded[:, 1:-1]
    right = jnp.concatenate([center[..., 1:], fill_right[..., None]], -1)
    left = jnp.concatenate([fill_left[..., None], center[..., :-1]], -1)
    return 4.0 * center - padded[:, 2:] - padded[:, :-2] - right - left


def sweeps(rhs, initial, region, base_table, term_table, galerkin, block_mask, block_inverse):
    terms = galerkin.shape[0]
    modes_all = galerkin.shape[1]
    blocks = block_mask.shape[1]
    width = modes_all // blocks
    shaped = galerkin.reshape(terms, blocks, width, blocks, width)
    coupling = (shaped * block_mask[:, :, None, :, None].astype(jnp.bfloat16)).reshape(
        terms, modes_all, modes_all
    )
    coupling = coupling.transpose(1, 0, 2).reshape(modes_all, terms * modes_all)

    fields, modes_dev = rhs.shape[:2]
    rows, cols = region.shape
    devs = lax.axis_size("modes")
    spaces = lax.axis_size("space")
    col_chunks = cols // LANES
    row_chunks = devs // col_chunks
    rows_c = rows // row_chunks
    me = lax.axis_index("modes")
    my_r = me // col_chunks
    my_c = me % col_chunks

    inv_hi = lax.optimization_barrier(block_inverse[0].astype(jnp.bfloat16))
    rest = block_inverse[0] - inv_hi.astype(jnp.float32)
    inv_mid = lax.optimization_barrier(rest.astype(jnp.bfloat16))
    inv_lo = (rest - inv_mid.astype(jnp.float32)).astype(jnp.bfloat16)
    inv_code = jnp.concatenate([inv_hi, inv_mid, inv_lo], axis=-1)

    base = lax.dynamic_slice(
        lookup(base_table, region), (0, my_r * rows_c, my_c * LANES), (fields, rows_c, LANES)
    )[:, :, None, :]
    coef = lax.dynamic_slice(
        lookup(term_table, region),
        (0, 0, my_r * rows_c, my_c * LANES),
        (fields, terms, rows_c, LANES),
    )
    coef = coef.transpose(0, 2, 1, 3)[:, :, :, None, :]
    inverse_base = 1.0 / (4.0 * base)

    rp = rhs.reshape(fields, modes_dev, row_chunks, rows_c, col_chunks, LANES)
    rp = rp.transpose(2, 4, 0, 3, 1, 5).reshape(devs, fields, rows_c, modes_dev, LANES)
    rhs_c = lax.all_to_all(rp, "modes", split_axis=0, concat_axis=3, tiled=True)[0]
    rhs_c = rhs_c.astype(jnp.float32)

    init_x = ring_halo(initial.transpose(0, 2, 1, 3), "space", 1)

    flat = ("space", "modes")
    total_rc = spaces * row_chunks

    def dev_of(g, c):
        s, r = divmod(g % total_rc, row_chunks)
        return s * devs + r * col_chunks + c

    down = [(dev_of(g, c), dev_of(g + 1, c)) for g in range(total_rc) for c in range(col_chunks)]
    up = [(b, a) for a, b in down]
    rightward = [
        (s * devs + r * col_chunks + c, s * devs + r * col_chunks + c + 1)
        for s in range(spaces)
        for r in range(row_chunks)
        for c in range(col_chunks - 1)
    ]
    leftward = [(b, a) for a, b in rightward]

    def pack(init_f):
        top = init_f[:, 0 : rows : rows_c]
        mid = init_f[:, 1 : rows + 1].reshape(fields, row_chunks, rows_c, modes_dev, cols)
        bot = init_f[:, rows_c + 1 : rows + 2 : rows_c]
        main = jnp.concatenate([top[:, :, None], mid, bot[:, :, None]], axis=2)
        main = main.reshape(fields, row_chunks, rows_c + 2, modes_dev, col_chunks, LANES)
        inner = init_f[:, 1 : rows + 1]
        hl = jnp.pad(inner[..., LANES - 1 : cols - 1 : LANES], ((0, 0), (0, 0), (0, 0), (1, 0)))
        hr = jnp.pad(inner[..., LANES : cols : LANES], ((0, 0), (0, 0), (0, 0), (0, 1)))
        sides = []
        for h in (hl, hr):
            h = h.reshape(fields, row_chunks, rows_c, modes_dev, col_chunks)
            sides.append(h.transpose(0, 1, 3, 4, 2))
        code = jnp.broadcast_to(
            inv_code[None, None, :, None, :], sides[0].shape[:-1] + inv_code.shape[-1:]
        )
        side = jnp.concatenate(sides + [code], axis=-1)
        side = jnp.pad(side, ((0, 0),) * 4 + ((0, LANES - side.shape[-1]),))[:, :, None]
        full = jnp.concatenate([main, side], axis=2)
        full = full.transpose(1, 4, 0, 2, 3, 5).reshape(devs, fields, -1, modes_dev, LANES)
        return lax.all_to_all(full, "modes", split_axis=0, concat_axis=3, tiled=True)[0]

    got = pack(init_x)
    padded = got[:, : rows_c + 2].astype(jnp.float32)
    side = got[:, rows_c + 2].astype(jnp.float32)
    fill_l = side[..., :rows_c].transpose(0, 2, 1)
    fill_r = side[..., rows_c : 2 * rows_c].transpose(0, 2, 1)
    code = side[0, :, 2 * rows_c : 2 * rows_c + 3 * width]
    every = (code[:, :width] + code[:, width : 2 * width]) + code[:, 2 * width :]
    every = every.reshape(blocks, width, width)
    eye = jnp.eye(blocks, dtype=jnp.float32)
    dense_inv = (every[:, :, None, :] * eye[:, None, :, None]).reshape(modes_all, modes_all)
    u_field = padded[:, 1:-1]

    def to_owner(mixed):
        mixed = mixed.reshape(fields, rows_c, devs, modes_dev, LANES)
        back = lax.all_to_all(mixed, "modes", split_axis=2, concat_axis=2, tiled=True)
        back = back.reshape(fields, rows_c, row_chunks, col_chunks, modes_dev, LANES)
        return back.transpose(0, 4, 2, 1, 3, 5).reshape(fields, modes_dev, rows, cols)

    coupled_owner = []
    for sweep in range(SWEEPS):
        if sweep > 0:
            low = lax.ppermute(u_field[:, -1:], flat, down)
            high = lax.ppermute(u_field[:, :1], flat, up)
            fill_l = lax.ppermute(u_field[..., -1], flat, rightward)
            fill_r = lax.ppermute(u_field[..., 0], flat, leftward)
            padded = jnp.concatenate([low, u_field, high], axis=1)
            rounded = lax.optimization_barrier(
                (padded.astype(jnp.bfloat16), fill_l.astype(jnp.bfloat16), fill_r.astype(jnp.bfloat16))
            )
            lap_r = laplace_rows(*(part.astype(jnp.float32) for part in rounded))
        else:
            lap = laplace_rows(padded, fill_l, fill_r)
            lap_r = lap
        tiles = (coef * lap_r[:, :, None]).astype(jnp.bfloat16)
        tiles = tiles.reshape(fields, rows_c, terms * modes_all, LANES)
        coupled = jnp.einsum(
            "ic,fxcy->fxiy", coupling, tiles, preferred_element_type=jnp.float32
        ).astype(jnp.bfloat16)
        coupled_owner.append(to_owner(coupled))
        if sweep < SWEEPS - 1:
            resid = rhs_c - base * lap - coupled.astype(jnp.float32)
            scaled = resid * inverse_base
            update = jnp.einsum(
                "ij,fxjy->fxiy", dense_inv, scaled, precision=lax.Precision.HIGHEST
            )
            u_field = u_field + 0.6 * update

    base_o = lookup(base_table, region)[:, None]
    inv_base_o = 1.0 / (4.0 * base_o)
    rhs_o = rhs.astype(jnp.float32)
    own_inv = block_inverse[0]
    pad_o = init_x.transpose(0, 2, 1, 3).astype(jnp.float32)
    u_o = pad_o[:, :, 1:-1]
    zeros = jnp.zeros(u_o.shape[:-1] + (1,), jnp.float32)
    for sweep in range(SWEEPS):
        if sweep > 0:
            pad_o = ring_halo(u_o, "space", 2)
        center = pad_o[:, :, 1:-1]
        right = jnp.concatenate([center[..., 1:], zeros], -1)
        left = jnp.concatenate([zeros, center[..., :-1]], -1)
        lap_o = 4.0 * center - pad_o[:, :, 2:] - pad_o[:, :, :-2] - right - left
        resid = rhs_o - base_o * lap_o - coupled_owner[sweep].astype(jnp.float32)
        scaled = resid * inv_base_o
        update = jnp.sum(own_inv[None, :, :, None, None] * scaled[:, None], axis=2)
        u_o = u_o + 0.6 * update
    return u_o


def solution(mesh):
    in_specs = (
        P(None, "modes", "space", None),
        P(None, "modes", "space", None),
        P("space", None),
        P(),
        P(),
        P(),
        P(),
        P("modes", None, None),
    )
    out_specs = P(None, "modes", "space", None)
    return jax.shard_map(sweeps, mesh=mesh, in_specs=in_specs, out_specs=out_specs, check_vma=False)
```

```python
import jax
import jax.numpy as jnp
from jax import lax
from jax.sharding import PartitionSpec as P

SWEEPS = 2
LANES = 128


def ring_halo(block, axis, dim):
    count = lax.axis_size(axis)
    forward = [(i, (i + 1) % count) for i in range(count)]
    backward = [(target, source) for source, target in forward]
    low = lax.ppermute(lax.slice_in_dim(block, block.shape[dim] - 1, None, axis=dim), axis, forward)
    high = lax.ppermute(lax.slice_in_dim(block, 0, 1, axis=dim), axis, backward)
    return jnp.concatenate([low, block, high], axis=dim)


def lookup(table, region):
    total = jnp.zeros(table.shape[:-1] + region.shape, jnp.float32)
    for which in range(table.shape[-1]):
        total = total + table[..., which, None, None] * (region == which).astype(jnp.float32)
    return total


def laplace_rows(padded, fill_left, fill_right):
    center = padded[:, 1:-1]
    right = jnp.concatenate([center[..., 1:], fill_right[..., None]], -1)
    left = jnp.concatenate([fill_left[..., None], center[..., :-1]], -1)
    return 4.0 * center - padded[:, 2:] - padded[:, :-2] - right - left


def sweeps(rhs, initial, region, base_table, term_table, galerkin, block_mask, block_inverse):
    terms = galerkin.shape[0]
    modes_all = galerkin.shape[1]
    blocks = block_mask.shape[1]
    width = modes_all // blocks
    shaped = galerkin.reshape(terms, blocks, width, blocks, width)
    coupling = (shaped * block_mask[:, :, None, :, None].astype(jnp.bfloat16)).reshape(
        terms, modes_all, modes_all
    )
    coupling = coupling.transpose(1, 0, 2).reshape(modes_all, terms * modes_all)

    fields, modes_dev = rhs.shape[:2]
    rows, cols = region.shape
    devs = lax.axis_size("modes")
    spaces = lax.axis_size("space")
    col_chunks = cols // LANES
    row_chunks = devs // col_chunks
    rows_c = rows // row_chunks
    me = lax.axis_index("modes")
    my_r = me // col_chunks
    my_c = me % col_chunks

    inv_hi = lax.optimization_barrier(block_inverse[0].astype(jnp.bfloat16))
    rest = block_inverse[0] - inv_hi.astype(jnp.float32)
    inv_mid = lax.optimization_barrier(rest.astype(jnp.bfloat16))
    inv_lo = (rest - inv_mid.astype(jnp.float32)).astype(jnp.bfloat16)
    inv_code = jnp.concatenate([inv_hi, inv_mid, inv_lo], axis=-1)

    base = lax.dynamic_slice(
        lookup(base_table, region), (0, my_r * rows_c, my_c * LANES), (fields, rows_c, LANES)
    )[:, :, None, :]
    coef = lax.dynamic_slice(
        lookup(term_table, region),
        (0, 0, my_r * rows_c, my_c * LANES),
        (fields, terms, rows_c, LANES),
    )
    coef = coef.transpose(0, 2, 1, 3)[:, :, :, None, :]
    inverse_base = 1.0 / (4.0 * base)

    rp = rhs.reshape(fields, modes_dev, row_chunks, rows_c, col_chunks, LANES)
    rp = rp.transpose(2, 4, 0, 3, 1, 5).reshape(devs, fields, rows_c, modes_dev, LANES)
    rhs_c = lax.all_to_all(rp, "modes", split_axis=0, concat_axis=3, tiled=True)[0]
    rhs_c = rhs_c.astype(jnp.float32)

    init_x = ring_halo(initial.transpose(0, 2, 1, 3), "space", 1)

    flat = ("space", "modes")
    total_rc = spaces * row_chunks

    def dev_of(g, c):
        s, r = divmod(g % total_rc, row_chunks)
        return s * devs + r * col_chunks + c

    down = [(dev_of(g, c), dev_of(g + 1, c)) for g in range(total_rc) for c in range(col_chunks)]
    up = [(b, a) for a, b in down]
    rightward = [
        (s * devs + r * col_chunks + c, s * devs + r * col_chunks + c + 1)
        for s in range(spaces)
        for r in range(row_chunks)
        for c in range(col_chunks - 1)
    ]
    leftward = [(b, a) for a, b in rightward]

    def pack(init_f):
        main = init_f.reshape(fields, row_chunks, rows_c, modes_dev, col_chunks, LANES)
        hl = jnp.pad(init_f[..., LANES - 1 : cols - 1 : LANES], ((0, 0), (0, 0), (0, 0), (1, 0)))
        hr = jnp.pad(init_f[..., LANES : cols : LANES], ((0, 0), (0, 0), (0, 0), (0, 1)))
        sides = []
        for h in (hl, hr):
            h = h.reshape(fields, row_chunks, rows_c, modes_dev, col_chunks)
            sides.append(h.transpose(0, 1, 3, 4, 2))
        code = jnp.broadcast_to(
            inv_code[None, None, :, None, :], sides[0].shape[:-1] + inv_code.shape[-1:]
        )
        side = jnp.concatenate(sides + [code], axis=-1)
        side = jnp.pad(side, ((0, 0),) * 4 + ((0, LANES - side.shape[-1]),))[:, :, None]
        full = jnp.concatenate([main, side], axis=2)
        full = full.transpose(1, 4, 0, 2, 3, 5).reshape(devs, fields, -1, modes_dev, LANES)
        return lax.all_to_all(full, "modes", split_axis=0, concat_axis=3, tiled=True)[0]

    got = pack(initial.transpose(0, 2, 1, 3))
    inner0 = got[:, :rows_c]
    low0 = lax.ppermute(inner0[:, -1:], flat, down)
    high0 = lax.ppermute(inner0[:, :1], flat, up)
    padded = jnp.concatenate([low0, inner0, high0], axis=1).astype(jnp.float32)
    side = got[:, rows_c].astype(jnp.float32)
    fill_l = side[..., :rows_c].transpose(0, 2, 1)
    fill_r = side[..., rows_c : 2 * rows_c].transpose(0, 2, 1)
    code = side[0, :, 2 * rows_c : 2 * rows_c + 3 * width]
    every = (code[:, :width] + code[:, width : 2 * width]) + code[:, 2 * width :]
    every = every.reshape(blocks, width, width)
    eye = jnp.eye(blocks, dtype=jnp.float32)
    dense_inv = (every[:, :, None, :] * eye[:, None, :, None]).reshape(modes_all, modes_all)
    u_field = padded[:, 1:-1]

    def to_owner(mixed):
        mixed = mixed.reshape(fields, rows_c, devs, modes_dev, LANES)
        back = lax.all_to_all(mixed, "modes", split_axis=2, concat_axis=2, tiled=True)
        back = back.reshape(fields, rows_c, row_chunks, col_chunks, modes_dev, LANES)
        return back.transpose(0, 4, 2, 1, 3, 5).reshape(fields, modes_dev, rows, cols)

    coupled_owner = []
    for sweep in range(SWEEPS):
        if sweep > 0:
            low = lax.ppermute(u_field[:, -1:], flat, down)
            high = lax.ppermute(u_field[:, :1], flat, up)
            fill_l = lax.ppermute(u_field[..., -1], flat, rightward)
            fill_r = lax.ppermute(u_field[..., 0], flat, leftward)
            padded = jnp.concatenate([low, u_field, high], axis=1)
            rounded = lax.optimization_barrier(
                (padded.astype(jnp.bfloat16), fill_l.astype(jnp.bfloat16), fill_r.astype(jnp.bfloat16))
            )
            lap_r = laplace_rows(*(part.astype(jnp.float32) for part in rounded))
        else:
            lap = laplace_rows(padded, fill_l, fill_r)
            lap_r = lap
        tiles = (coef * lap_r[:, :, None]).astype(jnp.bfloat16)
        tiles = tiles.reshape(fields, rows_c, terms * modes_all, LANES)
        coupled = jnp.einsum(
            "ic,fxcy->fxiy", coupling, tiles, preferred_element_type=jnp.float32
        ).astype(jnp.bfloat16)
        coupled_owner.append(to_owner(coupled))
        if sweep < SWEEPS - 1:
            resid = rhs_c - base * lap - coupled.astype(jnp.float32)
            scaled = resid * inverse_base
            update = jnp.einsum(
                "ij,fxjy->fxiy", dense_inv, scaled, precision=lax.Precision.HIGHEST
            )
            u_field = u_field + 0.6 * update

    base_o = lookup(base_table, region)[:, None]
    inv_base_o = 1.0 / (4.0 * base_o)
    rhs_o = rhs.astype(jnp.float32)
    own_inv = block_inverse[0]
    pad_o = init_x.transpose(0, 2, 1, 3).astype(jnp.float32)
    u_o = pad_o[:, :, 1:-1]
    zeros = jnp.zeros(u_o.shape[:-1] + (1,), jnp.float32)
    for sweep in range(SWEEPS):
        if sweep > 0:
            pad_o = ring_halo(u_o, "space", 2)
        center = pad_o[:, :, 1:-1]
        right = jnp.concatenate([center[..., 1:], zeros], -1)
        left = jnp.concatenate([zeros, center[..., :-1]], -1)
        lap_o = 4.0 * center - pad_o[:, :, 2:] - pad_o[:, :, :-2] - right - left
        resid = rhs_o - base_o * lap_o - coupled_owner[sweep].astype(jnp.float32)
        scaled = resid * inv_base_o
        update = jnp.einsum("ac,fcxy->faxy", own_inv, scaled, precision=lax.Precision.HIGHEST)
        u_o = u_o + 0.6 * update
    return u_o


def solution(mesh):
    in_specs = (
        P(None, "modes", "space", None),
        P(None, "modes", "space", None),
        P("space", None),
        P(),
        P(),
        P(),
        P(),
        P("modes", None, None),
    )
    out_specs = P(None, "modes", "space", None)
    return jax.shard_map(sweeps, mesh=mesh, in_specs=in_specs, out_specs=out_specs, check_vma=False)
```
